256 devices in a mesh: prow: 16 (over z, core), pcol: 16 (over y, x).
Axes of the slice: x: 4, y: 4, z: 8, core: 2. Of those that a mesh axis runs over, the one named last changes fastest.
Arguments:
- kernel: float32 [3, 16, 256, 3, 16, 256], P(None, 'prow', None, None, 'pcol'), as said below
Outputs:
- factored: float32 [3, 16, 256, 3, 16, 256], P(None, 'prow', None, None, 'pcol')
Inputs may be any that keep to these rules, and one draw needn't show every extreme that they name: kernel is symmetric (entry (a, b) equals entry (b, a)); every diagonal entry is 1.1, every off-diagonal entry lies in (0, 1], and the matrix is positive definite with smallest eigenvalue at least 0.1.
All inputs are finite; a program needn't handle non-finite values.
Results may differ from the reference program's by a relative error of at most 0.0003.
Values sent between devices are 32-bit elements; how exact they have to be, the bound alone decides.
No kernel may reach another device: no remote copies, remote signals or barrier semaphores. Data moves between devices by JAX's collectives and lax.ppermute only.
A program may use at most 64 MiB of HBM per device.

```python
import jax
import jax.numpy as jnp
from jax import lax

NMAT = 12288
BLK = 256
STEPS = 2
LBR = 3
LBC = 3


def draw_kernel(key, part):
    feature_count = 8
    positions = jax.random.normal(key, (NMAT, feature_count), jnp.float32)
    squared = jnp.zeros((NMAT, NMAT), jnp.float32)
    for column in range(feature_count):
        coordinate = positions[:, column]
        difference = coordinate[:, None] - coordinate[None, :]
        squared = squared + difference * difference
    kernel_vals = jnp.exp(squared * (-1.0 / feature_count))
    counter = jnp.arange(NMAT, dtype=jnp.int32)
    on_diag = counter[:, None] == counter[None, :]
    full = kernel_vals + jnp.where(on_diag, 0.1, 0.0).astype(jnp.float32)
    return full.reshape(LBR, NMAT // (LBR * BLK), BLK, LBC, NMAT // (LBC * BLK), BLK)


def setup_inputs(seed: int = 0) -> dict:
    keys = jax.random.split(jax.random.key(seed), 2)
    kernel = draw_kernel(jax.random.fold_in(keys[1], 71), 0)
    return {"kernel": kernel}


def reference(kernel):
    full = kernel.reshape(NMAT, NMAT)
    eye = jnp.eye(BLK, dtype=full.dtype)
    for k in range(STEPS):
        low = k * BLK
        high = low + BLK
        lower = jnp.linalg.cholesky(full[low:high, low:high])
        inverse = jax.scipy.linalg.solve_triangular(lower, eye, lower=True)
        product = jnp.dot(full[high:, low:high], inverse.T, precision=lax.Precision.HIGHEST)
        trailing = full[high:, high:] - jnp.dot(product, product.T, precision=lax.Precision.HIGHEST)
        full = full.at[low:high, low:high].set(lower)
        full = full.at[high:, low:high].set(product)
        full = full.at[low:high, high:].set(0.0)
        full = full.at[high:, high:].set(trailing)
    return full.reshape(kernel.shape)
```

```python
import jax
import jax.numpy as jnp
from jax import lax
from jax.sharding import PartitionSpec as P

HIGH = lax.Precision.HIGHEST


def chol_and_inverse(block, eye):
    lower = jnp.linalg.cholesky(block)
    inverse = jax.scipy.linalg.solve_triangular(lower, eye, lower=True)
    return lower, inverse


def on_device(kernel):
    prow = lax.axis_index("prow")
    pcol = lax.axis_index("pcol")
    rows = lax.axis_size("prow")
    cols = lax.axis_size("pcol")
    lbr, blk, lbc = kernel.shape[0], kernel.shape[2], kernel.shape[3]
    work = kernel.reshape(lbr, blk, lbc, blk)
    eye = jnp.eye(blk, dtype=jnp.float32)
    zero = jnp.zeros((blk, blk), jnp.float32)

    corner_blk = work[0, :, 0, :]
    slots = jnp.stack(
        [
            jnp.where((prow == 0) & (pcol == 0), corner_blk, zero),
            jnp.where((prow == 1) & (pcol == 0), corner_blk, zero),
            jnp.where((prow == 1) & (pcol == 1), corner_blk, zero),
        ]
    )
    corner = lax.psum(slots, ("prow", "pcol"))

    own_col = work[:, :, 0, :]
    row_slots = jnp.stack(
        [jnp.where(pcol == 0, own_col, 0.0), jnp.where(pcol == 1, own_col, 0.0)]
    )
    row_panel = lax.psum(row_slots, "pcol")

    own_row = work[0]
    col_slots = jnp.stack(
        [jnp.where(prow == 0, own_row, 0.0), jnp.where(prow == 1, own_row, 0.0)]
    )
    col_panel = lax.psum(col_slots, "prow")

    l0, w0 = chol_and_inverse(corner[0], eye)
    p10 = jnp.dot(corner[1], w0.T, precision=HIGH)
    s11 = corner[2] - jnp.dot(p10, p10.T, precision=HIGH)
    l1, w1 = chol_and_inverse(s11, eye)

    r0 = jnp.einsum("aik,jk->aij", row_panel[0], w0, precision=HIGH)
    r1 = row_panel[1] - jnp.einsum("aik,jk->aij", r0, p10, precision=HIGH)
    r1 = jnp.einsum("aik,jk->aij", r1, w1, precision=HIGH)

    c0t = jnp.einsum("ik,kbj->bij", w0, col_panel[0], precision=HIGH)
    c1t = jnp.transpose(col_panel[1], (1, 0, 2)) - jnp.einsum(
        "ik,bkj->bij", p10, c0t, precision=HIGH
    )
    c1t = jnp.einsum("ik,bkj->bij", w1, c1t, precision=HIGH)

    left = jnp.concatenate([r0, r1], axis=2)
    right = jnp.concatenate([c0t, c1t], axis=1)
    trailing = work - jnp.einsum("aik,bkj->aibj", left, right, precision=HIGH)

    row_ids = jnp.arange(lbr, dtype=jnp.int32) * rows + prow
    col_ids = jnp.arange(lbc, dtype=jnp.int32) * cols + pcol
    ri = row_ids[:, None, None, None]
    cj = col_ids[None, None, :, None]
    rk = row_ids[:, None, None]
    col0 = jnp.where(rk == 0, l0[None], r0)[:, :, None, :]
    col1 = jnp.where(rk == 0, 0.0, jnp.where(rk == 1, l1[None], r1))[:, :, None, :]
    out = jnp.where(cj == 0, col0, jnp.where(cj == 1, col1, trailing))
    out = jnp.where((ri < 2) & (cj > ri), 0.0, out)
    return out.reshape(kernel.shape)


def solution(mesh):
    spec = P(None, "prow", None, None, "pcol", None)
    return jax.shard_map(
        on_device, mesh=mesh, in_specs=(spec,), out_specs=spec, check_vma=False
    )
```

```python
import jax
import jax.numpy as jnp
from jax import lax
from jax.sharding import PartitionSpec as P

HIGH = lax.Precision.HIGHEST


def chol_and_inverse(block, eye):
    lower = jnp.linalg.cholesky(block)
    inverse = jax.scipy.linalg.solve_triangular(lower, eye, lower=True)
    return lower, inverse


def broadcast_from(x, axis, source):
    size = lax.axis_size(axis)
    rel = (lax.axis_index(axis) - source) % size
    have = jnp.where(rel == 0, x, 0.0)
    step = 1
    while step < size:
        pairs = [((source + i) % size, (source + i + step) % size) for i in range(step) if i + step < size]
        have = have + lax.ppermute(have, axis, pairs)
        step *= 2
    return have


def transposed(x, rows, cols):
    pairs = [(q * cols + p, p * cols + q) for p in range(rows) for q in range(cols) if p != q]
    moved = lax.ppermute(x, ("prow", "pcol"), pairs)
    same = lax.axis_index("prow") == lax.axis_index("pcol")
    return jnp.where(same, x, moved)


def on_device(kernel):
    prow = lax.axis_index("prow")
    pcol = lax.axis_index("pcol")
    rows = lax.axis_size("prow")
    cols = lax.axis_size("pcol")
    lbr, blk, lbc = kernel.shape[0], kernel.shape[2], kernel.shape[3]
    work = kernel.reshape(lbr, blk, lbc, blk)
    eye = jnp.eye(blk, dtype=jnp.float32)

    first = work[0, :, 0, :]
    m00 = broadcast_from(broadcast_from(first, "pcol", 0), "prow", 0)
    along0 = broadcast_from(first, "pcol", 0)
    along1 = broadcast_from(first, "pcol", 1)
    m10_m11 = broadcast_from(jnp.stack([along0, along1]), "prow", 1)

    x0 = broadcast_from(work[:, :, 0, :], "pcol", 0)
    x1 = broadcast_from(work[:, :, 0, :], "pcol", 1)

    l0, w0 = chol_and_inverse(m00, eye)
    p10 = jnp.dot(m10_m11[0], w0.T, precision=HIGH)
    s11 = m10_m11[1] - jnp.dot(p10, p10.T, precision=HIGH)
    l1, w1 = chol_and_inverse(s11, eye)

    r0 = jnp.einsum("aik,jk->aij", x0, w0, precision=HIGH)
    r1 = x1 - jnp.einsum("aik,jk->aij", r0, p10, precision=HIGH)
    r1 = jnp.einsum("aik,jk->aij", r1, w1, precision=HIGH)

    left = jnp.concatenate([r0, r1], axis=2)
    right = transposed(left, rows, cols)
    trailing = work - jnp.einsum("aik,bjk->aibj", left, right, precision=HIGH)

    row_ids = jnp.arange(lbr, dtype=jnp.int32) * rows + prow
    col_ids = jnp.arange(lbc, dtype=jnp.int32) * cols + pcol
    ri = row_ids[:, None, None, None]
    cj = col_ids[None, None, :, None]
    rk = row_ids[:, None, None]
    col0 = jnp.where(rk == 0, l0[None], r0)[:, :, None, :]
    col1 = jnp.where(rk == 0, 0.0, jnp.where(rk == 1, l1[None], r1))[:, :, None, :]
    out = jnp.where(cj == 0, col0, jnp.where(cj == 1, col1, trailing))
    out = jnp.where((ri < 2) & (cj > ri), 0.0, out)
    return out.reshape(kernel.shape)


def solution(mesh):
    spec = P(None, "prow", None, None, "pcol", None)
    return jax.shard_map(
        on_device, mesh=mesh, in_specs=(spec,), out_specs=spec, check_vma=False
    )
```

```python
import jax
import jax.numpy as jnp
from jax import lax
from jax.sharding import PartitionSpec as P

HIGH = lax.Precision.HIGHEST


def chol_and_inverse(block, eye):
    lower = jnp.linalg.cholesky(block)
    inverse = jax.scipy.linalg.solve_triangular(lower, eye, lower=True)
    return lower, inverse


def from_two_sources(own, axis, sources):
    peers = lax.axis_size(axis)
    shape = own.shape
    flat = own.reshape(-1, shape[-1])
    spare = -flat.shape[0] % peers
    flat = jnp.pad(flat, [(0, spare), (0, 0)])
    pieces = flat.reshape(peers, -1, shape[-1])
    mine = lax.all_to_all(pieces, axis, 0, 0, tiled=False)
    kept = jnp.stack([mine[s] for s in sources])
    spread = lax.all_to_all(
        jnp.broadcast_to(kept[None], (peers, *kept.shape)), axis, 0, 0, tiled=False
    )
    whole = jnp.swapaxes(spread, 0, 1).reshape(len(sources), -1, shape[-1])
    whole = whole[:, : flat.shape[0] - spare]
    return whole.reshape(len(sources), *shape)


def on_device(kernel):
    prow = lax.axis_index("prow")
    pcol = lax.axis_index("pcol")
    rows = lax.axis_size("prow")
    cols = lax.axis_size("pcol")
    lbr, blk, lbc = kernel.shape[0], kernel.shape[2], kernel.shape[3]
    work = kernel.reshape(lbr, blk, lbc, blk)
    eye = jnp.eye(blk, dtype=jnp.float32)

    ytop = from_two_sources(work[0], "prow", (0, 1))
    y0c = ytop[0][:, 0, :]
    y1c = ytop[1][:, 0, :]
    extra = jnp.where(pcol == 0, jnp.stack([y0c, y1c]), jnp.stack([y1c, jnp.zeros_like(y1c)]))
    own = jnp.concatenate([work[:, :, 0, :], extra], axis=0)
    xs = from_two_sources(own, "pcol", (0, 1))
    x0 = xs[0][:lbr]
    x1 = xs[1][:lbr]
    m00 = xs[0][lbr]
    m10 = xs[0][lbr + 1]
    m11 = xs[1][lbr]

    l0, w0 = chol_and_inverse(m00, eye)
    p10 = jnp.dot(m10, w0.T, precision=HIGH)
    s11 = m11 - jnp.dot(p10, p10.T, precision=HIGH)
    l1, w1 = chol_and_inverse(s11, eye)

    r0 = jnp.einsum("aik,jk->aij", x0, w0, precision=HIGH)
    r1 = x1 - jnp.einsum("aik,jk->aij", r0, p10, precision=HIGH)
    r1 = jnp.einsum("aik,jk->aij", r1, w1, precision=HIGH)

    c0t = jnp.einsum("ik,kbj->bij", w0, ytop[0], precision=HIGH)
    c1t = jnp.transpose(ytop[1], (1, 0, 2)) - jnp.einsum(
        "ik,bkj->bij", p10, c0t, precision=HIGH
    )
    c1t = jnp.einsum("ik,bkj->bij", w1, c1t, precision=HIGH)

    left = jnp.concatenate([r0, r1], axis=2)
    right = jnp.concatenate([c0t, c1t], axis=1)
    trailing = work - jnp.einsum("aik,bkj->aibj", left, right, precision=HIGH)

    row_ids = jnp.arange(lbr, dtype=jnp.int32) * rows + prow
    col_ids = jnp.arange(lbc, dtype=jnp.int32) * cols + pcol
    ri = row_ids[:, None, None, None]
    cj = col_ids[None, None, :, None]
    rk = row_ids[:, None, None]
    col0 = jnp.where(rk == 0, l0[None], r0)[:, :, None, :]
    col1 = jnp.where(rk == 0, 0.0, jnp.where(rk == 1, l1[None], r1))[:, :, None, :]
    out = jnp.where(cj == 0, col0, jnp.where(cj == 1, col1, trailing))
    out = jnp.where((ri < 2) & (cj > ri), 0.0, out)
    return out.reshape(kernel.shape)


def solution(mesh):
    spec = P(None, "prow", None, None, "pcol", None)
    return jax.shard_map(
        on_device, mesh=mesh, in_specs=(spec,), out_specs=spec, check_vma=False
    )
```

```python
import jax
import jax.numpy as jnp
from jax import lax
from jax.sharding import PartitionSpec as P

HIGH = lax.Precision.HIGHEST


def chol_and_inverse(block, eye):
    h = block.shape[0] // 2
    small = eye[:h, :h]
    la = jnp.linalg.cholesky(block[:h, :h])
    wa = jax.scipy.linalg.solve_triangular(la, small, lower=True)
    lb = jnp.dot(block[h:, :h], wa.T, precision=HIGH)
    lc = jnp.linalg.cholesky(block[h:, h:] - jnp.dot(lb, lb.T, precision=HIGH))
    wc = jax.scipy.linalg.solve_triangular(lc, small, lower=True)
    wb = -jnp.dot(wc, jnp.dot(lb, wa, precision=HIGH), precision=HIGH)
    zero = jnp.zeros_like(small)
    lower = jnp.block([[la, zero], [lb, lc]])
    inverse = jnp.block([[wa, zero], [wb, wc]])
    return lower, inverse


def from_two_sources(own, axis, sources):
    peers = lax.axis_size(axis)
    shape = own.shape
    flat = own.reshape(-1, shape[-1])
    spare = -flat.shape[0] % peers
    flat = jnp.pad(flat, [(0, spare), (0, 0)])
    pieces = flat.reshape(peers, -1, shape[-1])
    mine = lax.all_to_all(pieces, axis, 0, 0, tiled=False)
    kept = jnp.stack([mine[s] for s in sources])
    spread = lax.all_to_all(
        jnp.broadcast_to(kept[None], (peers, *kept.shape)), axis, 0, 0, tiled=False
    )
    whole = jnp.swapaxes(spread, 0, 1).reshape(len(sources), -1, shape[-1])
    whole = whole[:, : flat.shape[0] - spare]
    return whole.reshape(len(sources), *shape)


def on_device(kernel):
    prow = lax.axis_index("prow")
    pcol = lax.axis_index("pcol")
    rows = lax.axis_size("prow")
    cols = lax.axis_size("pcol")
    lbr, blk, lbc = kernel.shape[0], kernel.shape[2], kernel.shape[3]
    work = kernel.reshape(lbr, blk, lbc, blk)
    eye = jnp.eye(blk, dtype=jnp.float32)

    ytop = from_two_sources(work[0], "prow", (0, 1))
    y0c = ytop[0][:, 0, :]
    y1c = ytop[1][:, 0, :]
    extra = jnp.where(pcol == 0, jnp.stack([y0c, y1c]), jnp.stack([y1c, jnp.zeros_like(y1c)]))
    own = jnp.concatenate([work[:, :, 0, :], extra], axis=0)
    xs = from_two_sources(own, "pcol", (0, 1))
    x0 = xs[0][:lbr]
    x1 = xs[1][:lbr]
    m00 = xs[0][lbr]
    m10 = xs[0][lbr + 1]
    m11 = xs[1][lbr]

    l0, w0 = chol_and_inverse(m00, eye)
    p10 = jnp.dot(m10, w0.T, precision=HIGH)
    s11 = m11 - jnp.dot(p10, p10.T, precision=HIGH)
    l1, w1 = chol_and_inverse(s11, eye)

    r0 = jnp.einsum("aik,jk->aij", x0, w0, precision=HIGH)
    r1 = x1 - jnp.einsum("aik,jk->aij", r0, p10, precision=HIGH)
    r1 = jnp.einsum("aik,jk->aij", r1, w1, precision=HIGH)

    c0t = jnp.einsum("ik,kbj->bij", w0, ytop[0], precision=HIGH)
    c1t = jnp.transpose(ytop[1], (1, 0, 2)) - jnp.einsum(
        "ik,bkj->bij", p10, c0t, precision=HIGH
    )
    c1t = jnp.einsum("ik,bkj->bij", w1, c1t, precision=HIGH)

    left = jnp.concatenate([r0, r1], axis=2)
    right = jnp.concatenate([c0t, c1t], axis=1)
    trailing = work - jnp.einsum("aik,bkj->aibj", left, right, precision=HIGH)

    row_ids = jnp.arange(lbr, dtype=jnp.int32) * rows + prow
    col_ids = jnp.arange(lbc, dtype=jnp.int32) * cols + pcol
    ri = row_ids[:, None, None, None]
    cj = col_ids[None, None, :, None]
    rk = row_ids[:, None, None]
    col0 = jnp.where(rk == 0, l0[None], r0)[:, :, None, :]
    col1 = jnp.where(rk == 0, 0.0, jnp.where(rk == 1, l1[None], r1))[:, :, None, :]
    out = jnp.where(cj == 0, col0, jnp.where(cj == 1, col1, trailing))
    out = jnp.where((ri < 2) & (cj > ri), 0.0, out)
    return out.reshape(kernel.shape)


def solution(mesh):
    spec = P(None, "prow", None, None, "pcol", None)
    return jax.shard_map(
        on_device, mesh=mesh, in_specs=(spec,), out_specs=spec, check_vma=False
    )
```

```python
import jax
import jax.numpy as jnp
from jax import lax
from jax.sharding import PartitionSpec as P

HIGH = lax.Precision.HIGHEST


def chol_and_inverse(block, eye):
    h = block.shape[0] // 2
    small = eye[:h, :h]
    la = jnp.linalg.cholesky(block[:h, :h], symmetrize_input=False)
    wa = jax.scipy.linalg.solve_triangular(la, small, lower=True)
    lb = jnp.dot(block[h:, :h], wa.T, precision=HIGH)
    lc = jnp.linalg.cholesky(
        block[h:, h:] - jnp.dot(lb, lb.T, precision=HIGH), symmetrize_input=False
    )
    wc = jax.scipy.linalg.solve_triangular(lc, small, lower=True)
    wb = -jnp.dot(wc, jnp.dot(lb, wa, precision=HIGH), precision=HIGH)
    zero = jnp.zeros_like(small)
    lower = jnp.block([[la, zero], [lb, lc]])
    inverse = jnp.block([[wa, zero], [wb, wc]])
    return lower, inverse


def from_two_sources(own, axis, sources):
    peers = lax.axis_size(axis)
    shape = own.shape
    flat = own.reshape(-1, shape[-1])
    spare = -flat.shape[0] % peers
    flat = jnp.pad(flat, [(0, spare), (0, 0)])
    pieces = flat.reshape(peers, -1, shape[-1])
    mine = lax.all_to_all(pieces, axis, 0, 0, tiled=False)
    kept = jnp.stack([mine[s] for s in sources])
    spread = lax.all_to_all(
        jnp.broadcast_to(kept[None], (peers, *kept.shape)), axis, 0, 0, tiled=False
    )
    whole = jnp.swapaxes(spread, 0, 1).reshape(len(sources), -1, shape[-1])
    whole = whole[:, : flat.shape[0] - spare]
    return whole.reshape(len(sources), *shape)


def on_device(kernel):
    prow = lax.axis_index("prow")
    pcol = lax.axis_index("pcol")
    rows = lax.axis_size("prow")
    cols = lax.axis_size("pcol")
    lbr, blk, lbc = kernel.shape[0], kernel.shape[2], kernel.shape[3]
    work = kernel.reshape(lbr, blk, lbc, blk)
    eye = jnp.eye(blk, dtype=jnp.float32)

    ytop = from_two_sources(work[0], "prow", (0, 1))
    y0c = ytop[0][:, 0, :]
    y1c = ytop[1][:, 0, :]
    extra = jnp.where(pcol == 0, jnp.stack([y0c, y1c]), jnp.stack([y1c, jnp.zeros_like(y1c)]))
    own = jnp.concatenate([work[:, :, 0, :], extra], axis=0)
    xs = from_two_sources(own, "pcol", (0, 1))
    x0 = xs[0][:lbr]
    x1 = xs[1][:lbr]
    m00 = xs[0][lbr]
    m10 = xs[0][lbr + 1]
    m11 = xs[1][lbr]

    l0, w0 = chol_and_inverse(m00, eye)
    p10 = jnp.dot(m10, w0.T, precision=HIGH)
    s11 = m11 - jnp.dot(p10, p10.T, precision=HIGH)
    l1, w1 = chol_and_inverse(s11, eye)

    r0 = jnp.einsum("aik,jk->aij", x0, w0, precision=HIGH)
    r1 = x1 - jnp.einsum("aik,jk->aij", r0, p10, precision=HIGH)
    r1 = jnp.einsum("aik,jk->aij", r1, w1, precision=HIGH)

    c0t = jnp.einsum("ik,kbj->bij", w0, ytop[0], precision=HIGH)
    c1t = jnp.transpose(ytop[1], (1, 0, 2)) - jnp.einsum(
        "ik,bkj->bij", p10, c0t, precision=HIGH
    )
    c1t = jnp.einsum("ik,bkj->bij", w1, c1t, precision=HIGH)

    left = jnp.concatenate([r0, r1], axis=2)
    right = jnp.concatenate([c0t, c1t], axis=1)
    trailing = work - jnp.einsum("aik,bkj->aibj", left, right, precision=HIGH)

    row_ids = jnp.arange(lbr, dtype=jnp.int32) * rows + prow
    col_ids = jnp.arange(lbc, dtype=jnp.int32) * cols + pcol
    rk = row_ids[:, None, None]
    col0 = jnp.where(rk == 0, l0[None], r0)
    col1 = jnp.where(rk == 0, 0.0, jnp.where(rk == 1, l1[None], r1))
    first_col = jnp.where(pcol == 0, col0, jnp.where(pcol == 1, col1, trailing[:, :, 0, :]))
    out = trailing.at[:, :, 0, :].set(first_col)
    upper = (prow < 2) & (col_ids > prow)
    out = out.at[0].set(jnp.where(upper[None, :, None], 0.0, out[0]))
    return out.reshape(kernel.shape)


def solution(mesh):
    spec = P(None, "prow", None, None, "pcol", None)
    return jax.shard_map(
        on_device, mesh=mesh, in_specs=(spec,), out_specs=spec, check_vma=False
    )
```

```python
import jax
import jax.numpy as jnp
from jax import lax
from jax.sharding import PartitionSpec as P

HIGH = lax.Precision.HIGHEST


def chol_and_inverse(block, eye):
    h = block.shape[0] // 2
    small = eye[:h, :h]
    la = jnp.linalg.cholesky(block[:h, :h], symmetrize_input=False)
    wa = jax.scipy.linalg.solve_triangular(la, small, lower=True)
    lb = jnp.dot(block[h:, :h], wa.T, precision=HIGH)
    lc = jnp.linalg.cholesky(
        block[h:, h:] - jnp.dot(lb, lb.T, precision=HIGH), symmetrize_input=False
    )
    wc = jax.scipy.linalg.solve_triangular(lc, small, lower=True)
    wb = -jnp.dot(wc, jnp.dot(lb, wa, precision=HIGH), precision=HIGH)
    zero = jnp.zeros_like(small)
    lower = jnp.block([[la, zero], [lb, lc]])
    inverse = jnp.block([[wa, zero], [wb, wc]])
    return lower, inverse


def from_two_sources(own, axis, sources):
    peers = lax.axis_size(axis)
    shape = own.shape
    flat = own.reshape(-1, shape[-1])
    spare = -flat.shape[0] % peers
    flat = jnp.pad(flat, [(0, spare), (0, 0)])
    pieces = flat.reshape(peers, -1, shape[-1])
    mine = lax.all_to_all(pieces, axis, 0, 0, tiled=False)
    kept = jnp.stack([mine[s] for s in sources])
    spread = lax.all_to_all(
        jnp.broadcast_to(kept[None], (peers, *kept.shape)), axis, 0, 0, tiled=False
    )
    whole = jnp.swapaxes(spread, 0, 1).reshape(len(sources), -1, shape[-1])
    whole = whole[:, : flat.shape[0] - spare]
    return whole.reshape(len(sources), *shape)


def on_device(kernel):
    prow = lax.axis_index("prow")
    pcol = lax.axis_index("pcol")
    rows = lax.axis_size("prow")
    cols = lax.axis_size("pcol")
    lbr, blk, lbc = kernel.shape[0], kernel.shape[2], kernel.shape[3]
    work = kernel.reshape(lbr, blk, lbc, blk)
    eye = jnp.eye(blk, dtype=jnp.float32)

    ytop = from_two_sources(work[0], "prow", (0, 1))
    y0c = ytop[0][:, 0, :]
    y1c = ytop[1][:, 0, :]
    extra = jnp.where(pcol == 0, jnp.stack([y0c, y1c]), jnp.stack([y1c, jnp.zeros_like(y1c)]))
    panel = work[:, :, 0, :].reshape(cols, -1, blk)
    extra_pieces = extra.reshape(cols, -1, blk)
    cut = panel.shape[1]
    pieces = jnp.concatenate([panel, extra_pieces], axis=1)
    mine = lax.all_to_all(pieces, "pcol", 0, 0, tiled=False)
    kept = jnp.stack([mine[0], mine[1]])
    spread = lax.all_to_all(
        jnp.broadcast_to(kept[None, :, cut:], (cols, 2, kept.shape[1] - cut, blk)),
        "pcol", 0, 0, tiled=False,
    )
    corner = jnp.swapaxes(spread, 0, 1).reshape(2, 2, blk, blk)
    m00 = corner[0, 0]
    m10 = corner[0, 1]
    m11 = corner[1, 0]
    gathered = lax.all_gather(kept[:, :cut], "pcol", axis=0, tiled=False)
    xs = jnp.swapaxes(gathered, 0, 1).reshape(2, lbr, blk, blk)
    x0 = xs[0]
    x1 = xs[1]

    l0, w0 = chol_and_inverse(m00, eye)
    p10 = jnp.dot(m10, w0.T, precision=HIGH)
    s11 = m11 - jnp.dot(p10, p10.T, precision=HIGH)
    l1, w1 = chol_and_inverse(s11, eye)

    r0 = jnp.einsum("aik,jk->aij", x0, w0, precision=HIGH)
    r1 = x1 - jnp.einsum("aik,jk->aij", r0, p10, precision=HIGH)
    r1 = jnp.einsum("aik,jk->aij", r1, w1, precision=HIGH)

    c0t = jnp.einsum("ik,kbj->bij", w0, ytop[0], precision=HIGH)
    c1t = jnp.transpose(ytop[1], (1, 0, 2)) - jnp.einsum(
        "ik,bkj->bij", p10, c0t, precision=HIGH
    )
    c1t = jnp.einsum("ik,bkj->bij", w1, c1t, precision=HIGH)

    left = jnp.concatenate([r0, r1], axis=2)
    right = jnp.concatenate([c0t, c1t], axis=1)
    trailing = work - jnp.einsum("aik,bkj->aibj", left, right, precision=HIGH)

    row_ids = jnp.arange(lbr, dtype=jnp.int32) * rows + prow
    col_ids = jnp.arange(lbc, dtype=jnp.int32) * cols + pcol
    rk = row_ids[:, None, None]
    col0 = jnp.where(rk == 0, l0[None], r0)
    col1 = jnp.where(rk == 0, 0.0, jnp.where(rk == 1, l1[None], r1))
    first_col = jnp.where(pcol == 0, col0, jnp.where(pcol == 1, col1, trailing[:, :, 0, :]))
    out = trailing.at[:, :, 0, :].set(first_col)
    upper = (prow < 2) & (col_ids > prow)
    out = out.at[0].set(jnp.where(upper[None, :, None], 0.0, out[0]))
    return out.reshape(kernel.shape)


def solution(mesh):
    spec = P(None, "prow", None, None, "pcol", None)
    return jax.shard_map(
        on_device, mesh=mesh, in_specs=(spec,), out_specs=spec, check_vma=False
    )
```

```python
import jax
import jax.numpy as jnp
from jax import lax
from jax.sharding import PartitionSpec as P

HIGH = lax.Precision.HIGHEST


def chol_and_inverse(block, eye):
    h = block.shape[0] // 2
    small = eye[:h, :h]
    la = jnp.linalg.cholesky(block[:h, :h], symmetrize_input=False)
    wa = jax.scipy.linalg.solve_triangular(la, small, lower=True)
    lb = jnp.dot(block[h:, :h], wa.T, precision=HIGH)
    lc = jnp.linalg.cholesky(
        block[h:, h:] - jnp.dot(lb, lb.T, precision=HIGH), symmetrize_input=False
    )
    wc = jax.scipy.linalg.solve_triangular(lc, small, lower=True)
    wb = -jnp.dot(wc, jnp.dot(lb, wa, precision=HIGH), precision=HIGH)
    zero = jnp.zeros_like(small)
    lower = jnp.block([[la, zero], [lb, lc]])
    inverse = jnp.block([[wa, zero], [wb, wc]])
    return lower, inverse


def from_two_sources(own, axis, sources):
    peers = lax.axis_size(axis)
    shape = own.shape
    flat = own.reshape(-1, shape[-1])
    spare = -flat.shape[0] % peers
    flat = jnp.pad(flat, [(0, spare), (0, 0)])
    pieces = flat.reshape(peers, -1, shape[-1])
    mine = lax.all_to_all(pieces, axis, 0, 0, tiled=False)
    kept = jnp.stack([mine[s] for s in sources])
    spread = lax.all_to_all(
        jnp.broadcast_to(kept[None], (peers, *kept.shape)), axis, 0, 0, tiled=False
    )
    whole = jnp.swapaxes(spread, 0, 1).reshape(len(sources), -1, shape[-1])
    whole = whole[:, : flat.shape[0] - spare]
    return whole.reshape(len(sources), *shape)


def on_device(kernel):
    prow = lax.axis_index("prow")
    pcol = lax.axis_index("pcol")
    rows = lax.axis_size("prow")
    cols = lax.axis_size("pcol")
    lbr, blk, lbc = kernel.shape[0], kernel.shape[2], kernel.shape[3]
    work = kernel.reshape(lbr, blk, lbc, blk)
    eye = jnp.eye(blk, dtype=jnp.float32)

    top = work[0]
    top_first = top[:, 0, :].reshape(rows, -1, blk)
    top_rest = jnp.swapaxes(top[:, 1:, :], 0, 1).reshape(rows, -1, blk)
    split = top_first.shape[1]
    top_mine = lax.all_to_all(
        jnp.concatenate([top_first, top_rest], axis=1), "prow", 0, 0, tiled=False
    )
    top_kept = jnp.stack([top_mine[0], top_mine[1]])
    top_spread = lax.all_to_all(
        jnp.broadcast_to(top_kept[None, :, :split], (rows, 2, split, blk)),
        "prow", 0, 0, tiled=False,
    )
    y_first = jnp.swapaxes(top_spread, 0, 1).reshape(2, blk, blk)
    y0c = y_first[0]
    y1c = y_first[1]
    top_gathered = lax.all_gather(top_kept[:, split:], "prow", axis=0, tiled=False)
    y_rest = jnp.swapaxes(top_gathered, 0, 1).reshape(2, lbc - 1, blk, blk)
    ytop = jnp.concatenate([y_first[:, None], y_rest], axis=1).transpose(0, 2, 1, 3)

    extra = jnp.where(pcol == 0, jnp.stack([y0c, y1c]), jnp.stack([y1c, jnp.zeros_like(y1c)]))
    panel = work[:, :, 0, :].reshape(cols, -1, blk)
    extra_pieces = extra.reshape(cols, -1, blk)
    cut = panel.shape[1]
    pieces = jnp.concatenate([panel, extra_pieces], axis=1)
    mine = lax.all_to_all(pieces, "pcol", 0, 0, tiled=False)
    kept = jnp.stack([mine[0], mine[1]])
    spread = lax.all_to_all(
        jnp.broadcast_to(kept[None, :, cut:], (cols, 2, kept.shape[1] - cut, blk)),
        "pcol", 0, 0, tiled=False,
    )
    corner = jnp.swapaxes(spread, 0, 1).reshape(2, 2, blk, blk)
    m00 = corner[0, 0]
    m10 = corner[0, 1]
    m11 = corner[1, 0]
    gathered = lax.all_gather(kept[:, :cut], "pcol", axis=0, tiled=False)
    xs = jnp.swapaxes(gathered, 0, 1).reshape(2, lbr, blk, blk)
    x0 = xs[0]
    x1 = xs[1]

    l0, w0 = chol_and_inverse(m00, eye)
    p10 = jnp.dot(m10, w0.T, precision=HIGH)
    s11 = m11 - jnp.dot(p10, p10.T, precision=HIGH)
    l1, w1 = chol_and_inverse(s11, eye)

    r0 = jnp.einsum("aik,jk->aij", x0, w0, precision=HIGH)
    r1 = x1 - jnp.einsum("aik,jk->aij", r0, p10, precision=HIGH)
    r1 = jnp.einsum("aik,jk->aij", r1, w1, precision=HIGH)

    c0t = jnp.einsum("ik,kbj->bij", w0, ytop[0], precision=HIGH)
    c1t = jnp.transpose(ytop[1], (1, 0, 2)) - jnp.einsum(
        "ik,bkj->bij", p10, c0t, precision=HIGH
    )
    c1t = jnp.einsum("ik,bkj->bij", w1, c1t, precision=HIGH)

    left = jnp.concatenate([r0, r1], axis=2)
    right = jnp.concatenate([c0t, c1t], axis=1)
    trailing = work - jnp.einsum("aik,bkj->aibj", left, right, precision=HIGH)

    row_ids = jnp.arange(lbr, dtype=jnp.int32) * rows + prow
    col_ids = jnp.arange(lbc, dtype=jnp.int32) * cols + pcol
    rk = row_ids[:, None, None]
    col0 = jnp.where(rk == 0, l0[None], r0)
    col1 = jnp.where(rk == 0, 0.0, jnp.where(rk == 1, l1[None], r1))
    first_col = jnp.where(pcol == 0, col0, jnp.where(pcol == 1, col1, trailing[:, :, 0, :]))
    out = trailing.at[:, :, 0, :].set(first_col)
    upper = (prow < 2) & (col_ids > prow)
    out = out.at[0].set(jnp.where(upper[None, :, None], 0.0, out[0]))
    return out.reshape(kernel.shape)


def solution(mesh):
    spec = P(None, "prow", None, None, "pcol", None)
    return jax.shard_map(
        on_device, mesh=mesh, in_specs=(spec,), out_specs=spec, check_vma=False
    )
```

```python
import jax
import jax.numpy as jnp
from jax import lax
from jax.sharding import PartitionSpec as P

HIGH = lax.Precision.HIGHEST


def chol_and_inverse(block, eye):
    h = block.shape[0] // 2
    small = eye[:h, :h]
    la = jnp.linalg.cholesky(block[:h, :h], symmetrize_input=False)
    wa = jax.scipy.linalg.solve_triangular(la, small, lower=True)
    lb = jnp.dot(block[h:, :h], wa.T, precision=HIGH)
    lc = jnp.linalg.cholesky(
        block[h:, h:] - jnp.dot(lb, lb.T, precision=HIGH), symmetrize_input=False
    )
    wc = jax.scipy.linalg.solve_triangular(lc, small, lower=True)
    wb = -jnp.dot(wc, jnp.dot(lb, wa, precision=HIGH), precision=HIGH)
    zero = jnp.zeros_like(small)
    lower = jnp.block([[la, zero], [lb, lc]])
    inverse = jnp.block([[wa, zero], [wb, wc]])
    return lower, inverse


def from_two_sources(own, axis, sources):
    peers = lax.axis_size(axis)
    shape = own.shape
    flat = own.reshape(-1, shape[-1])
    spare = -flat.shape[0] % peers
    flat = jnp.pad(flat, [(0, spare), (0, 0)])
    pieces = flat.reshape(peers, -1, shape[-1])
    mine = lax.all_to_all(pieces, axis, 0, 0, tiled=False)
    kept = jnp.stack([mine[s] for s in sources])
    spread = lax.all_to_all(
        jnp.broadcast_to(kept[None], (peers, *kept.shape)), axis, 0, 0, tiled=False
    )
    whole = jnp.swapaxes(spread, 0, 1).reshape(len(sources), -1, shape[-1])
    whole = whole[:, : flat.shape[0] - spare]
    return whole.reshape(len(sources), *shape)


def on_device(kernel):
    prow = lax.axis_index("prow")
    pcol = lax.axis_index("pcol")
    rows = lax.axis_size("prow")
    cols = lax.axis_size("pcol")
    lbr, blk, lbc = kernel.shape[0], kernel.shape[2], kernel.shape[3]
    work = kernel.reshape(lbr, blk, lbc, blk)
    eye = jnp.eye(blk, dtype=jnp.float32)

    first = from_two_sources(work[0, :, 0, :], "prow", (0, 1))
    extra = jnp.where(
        pcol == 0, first, jnp.stack([first[1], jnp.zeros_like(first[1])])
    )
    corner = from_two_sources(extra, "pcol", (0, 1))
    m00 = corner[0, 0]
    m10 = corner[0, 1]
    m11 = corner[1, 0]

    def offloaded(own, axis, owners):
        idx = lax.axis_index(axis)
        slots = jnp.stack([jnp.where(idx == s, own, 0.0) for s in owners])
        flat = slots.reshape(len(owners), -1, blk)
        part = lax.psum_scatter(flat, axis, scatter_dimension=1, tiled=True)
        return lax.all_gather(part, axis, axis=1, tiled=True).reshape(slots.shape)

    rest = offloaded(jnp.swapaxes(work[0][:, 1:, :], 0, 1), "prow", (0, 1))
    ytop = jnp.concatenate([first[:, None], rest], axis=1).transpose(0, 2, 1, 3)
    xs = offloaded(work[:, :, 0, :], "pcol", (0, 1))
    x0 = xs[0]
    x1 = xs[1]

    l0, w0 = chol_and_inverse(m00, eye)
    p10 = jnp.dot(m10, w0.T, precision=HIGH)
    s11 = m11 - jnp.dot(p10, p10.T, precision=HIGH)
    l1, w1 = chol_and_inverse(s11, eye)

    r0 = jnp.einsum("aik,jk->aij", x0, w0, precision=HIGH)
    r1 = x1 - jnp.einsum("aik,jk->aij", r0, p10, precision=HIGH)
    r1 = jnp.einsum("aik,jk->aij", r1, w1, precision=HIGH)

    c0t = jnp.einsum("ik,kbj->bij", w0, ytop[0], precision=HIGH)
    c1t = jnp.transpose(ytop[1], (1, 0, 2)) - jnp.einsum(
        "ik,bkj->bij", p10, c0t, precision=HIGH
    )
    c1t = jnp.einsum("ik,bkj->bij", w1, c1t, precision=HIGH)

    left = jnp.concatenate([r0, r1], axis=2)
    right = jnp.concatenate([c0t, c1t], axis=1)
    trailing = work - jnp.einsum("aik,bkj->aibj", left, right, precision=HIGH)

    row_ids = jnp.arange(lbr, dtype=jnp.int32) * rows + prow
    col_ids = jnp.arange(lbc, dtype=jnp.int32) * cols + pcol
    rk = row_ids[:, None, None]
    col0 = jnp.where(rk == 0, l0[None], r0)
    col1 = jnp.where(rk == 0, 0.0, jnp.where(rk == 1, l1[None], r1))
    first_col = jnp.where(pcol == 0, col0, jnp.where(pcol == 1, col1, trailing[:, :, 0, :]))
    out = trailing.at[:, :, 0, :].set(first_col)
    upper = (prow < 2) & (col_ids > prow)
    out = out.at[0].set(jnp.where(upper[None, :, None], 0.0, out[0]))
    return out.reshape(kernel.shape)


def solution(mesh):
    spec = P(None, "prow", None, None, "pcol", None)
    return jax.shard_map(
        on_device, mesh=mesh, in_specs=(spec,), out_specs=spec, check_vma=False
    )
```

```python
import jax
import jax.numpy as jnp
from jax import lax
from jax.sharding import PartitionSpec as P

HIGH = lax.Precision.HIGHEST


def chol_and_inverse(block, eye):
    h = block.shape[0] // 2
    small = eye[:h, :h]
    la = jnp.linalg.cholesky(block[:h, :h], symmetrize_input=False)
    wa = jax.scipy.linalg.solve_triangular(la, small, lower=True)
    lb = jnp.dot(block[h:, :h], wa.T, precision=HIGH)
    lc = jnp.linalg.cholesky(
        block[h:, h:] - jnp.dot(lb, lb.T, precision=HIGH), symmetrize_input=False
    )
    wc = jax.scipy.linalg.solve_triangular(lc, small, lower=True)
    wb = -jnp.dot(wc, jnp.dot(lb, wa, precision=HIGH), precision=HIGH)
    zero = jnp.zeros_like(small)
    lower = jnp.block([[la, zero], [lb, lc]])
    inverse = jnp.block([[wa, zero], [wb, wc]])
    return lower, inverse


def from_two_sources(own, axis, sources):
    peers = lax.axis_size(axis)
    shape = own.shape
    flat = own.reshape(-1, shape[-1])
    spare = -flat.shape[0] % peers
    flat = jnp.pad(flat, [(0, spare), (0, 0)])
    pieces = flat.reshape(peers, -1, shape[-1])
    mine = lax.all_to_all(pieces, axis, 0, 0, tiled=False)
    kept = jnp.stack([mine[s] for s in sources])
    spread = lax.all_to_all(
        jnp.broadcast_to(kept[None], (peers, *kept.shape)), axis, 0, 0, tiled=False
    )
    whole = jnp.swapaxes(spread, 0, 1).reshape(len(sources), -1, shape[-1])
    whole = whole[:, : flat.shape[0] - spare]
    return whole.reshape(len(sources), *shape)


def on_device(kernel):
    prow = lax.axis_index("prow")
    pcol = lax.axis_index("pcol")
    rows = lax.axis_size("prow")
    cols = lax.axis_size("pcol")
    lbr, blk, lbc = kernel.shape[0], kernel.shape[2], kernel.shape[3]
    work = kernel.reshape(lbr, blk, lbc, blk)
    eye = jnp.eye(blk, dtype=jnp.float32)

    top = work[0]
    top_first = top[:, 0, :].reshape(rows, -1, blk)
    top_rest = jnp.swapaxes(top[:, 1:, :], 0, 1).reshape(rows, -1, blk)
    split = top_first.shape[1]
    top_mine = lax.all_to_all(
        jnp.concatenate([top_first, top_rest], axis=1), "prow", 0, 0, tiled=False
    )
    top_kept = jnp.stack([top_mine[0], top_mine[1]])
    top_spread = lax.all_to_all(
        jnp.broadcast_to(top_kept[None, :, :split], (rows, 2, split, blk)),
        "prow", 0, 0, tiled=False,
    )
    y_first = jnp.swapaxes(top_spread, 0, 1).reshape(2, blk, blk)
    y0c = y_first[0]
    y1c = y_first[1]
    top_gathered = lax.all_gather(top_kept[:, split:], "prow", axis=0, tiled=False)
    y_rest = jnp.swapaxes(top_gathered, 0, 1).reshape(2, lbc - 1, blk, blk)
    ytop = jnp.concatenate([y_first[:, None], y_rest], axis=1)

    extra = jnp.where(pcol == 0, jnp.stack([y0c, y1c]), jnp.stack([y1c, jnp.zeros_like(y1c)]))
    panel = work[:, :, 0, :].reshape(cols, -1, blk)
    extra_pieces = extra.reshape(cols, -1, blk)
    cut = panel.shape[1]
    pieces = jnp.concatenate([panel, extra_pieces], axis=1)
    mine = lax.all_to_all(pieces, "pcol", 0, 0, tiled=False)
    kept = jnp.stack([mine[0], mine[1]])
    spread = lax.all_to_all(
        jnp.broadcast_to(kept[None, :, cut:], (cols, 2, kept.shape[1] - cut, blk)),
        "pcol", 0, 0, tiled=False,
    )
    corner = jnp.swapaxes(spread, 0, 1).reshape(2, 2, blk, blk)
    m00 = corner[0, 0]
    m10 = corner[0, 1]
    m11 = corner[1, 0]
    gathered = lax.all_gather(kept[:, :cut], "pcol", axis=0, tiled=False)
    xs = jnp.swapaxes(gathered, 0, 1).reshape(2, lbr, blk, blk)
    x0 = xs[0]
    x1 = xs[1]

    l0, w0 = chol_and_inverse(m00, eye)
    p10 = jnp.dot(m10, w0.T, precision=HIGH)
    s11 = m11 - jnp.dot(p10, p10.T, precision=HIGH)
    l1, w1 = chol_and_inverse(s11, eye)

    r0 = jnp.einsum("aik,jk->aij", x0, w0, precision=HIGH)
    r1 = x1 - jnp.einsum("aik,jk->aij", r0, p10, precision=HIGH)
    r1 = jnp.einsum("aik,jk->aij", r1, w1, precision=HIGH)

    c0t = jnp.einsum("ik,bkj->bij", w0, ytop[0], precision=HIGH)
    c1t = ytop[1] - jnp.einsum("ik,bkj->bij", p10, c0t, precision=HIGH)
    c1t = jnp.einsum("ik,bkj->bij", w1, c1t, precision=HIGH)

    left = jnp.concatenate([r0, r1], axis=2)
    right = jnp.concatenate([c0t, c1t], axis=1)
    trailing = work - jnp.einsum("aik,bkj->aibj", left, right, precision=HIGH)

    row_ids = jnp.arange(lbr, dtype=jnp.int32) * rows + prow
    col_ids = jnp.arange(lbc, dtype=jnp.int32) * cols + pcol
    rk = row_ids[:, None, None]
    col0 = jnp.where(rk == 0, l0[None], r0)
    col1 = jnp.where(rk == 0, 0.0, jnp.where(rk == 1, l1[None], r1))
    first_col = jnp.where(pcol == 0, col0, jnp.where(pcol == 1, col1, trailing[:, :, 0, :]))
    out = trailing.at[:, :, 0, :].set(first_col)
    upper = (prow < 2) & (col_ids > prow)
    out = out.at[0].set(jnp.where(upper[None, :, None], 0.0, out[0]))
    return out.reshape(kernel.shape)


def solution(mesh):
    spec = P(None, "prow", None, None, "pcol", None)
    return jax.shard_map(
        on_device, mesh=mesh, in_specs=(spec,), out_specs=spec, check_vma=False
    )
```

```python
import jax
import jax.numpy as jnp
from jax import lax
from jax.sharding import PartitionSpec as P

HIGH = lax.Precision.HIGHEST


def chol_and_inverse(block, eye):
    h = block.shape[0] // 2
    small = eye[:h, :h]
    la = jnp.linalg.cholesky(block[:h, :h], symmetrize_input=False)
    wa = jax.scipy.linalg.solve_triangular(la, small, lower=True)
    lb = jnp.dot(block[h:, :h], wa.T, precision=HIGH)
    lc = jnp.linalg.cholesky(
        block[h:, h:] - jnp.dot(lb, lb.T, precision=HIGH), symmetrize_input=False
    )
    wc = jax.scipy.linalg.solve_triangular(lc, small, lower=True)
    wb = -jnp.dot(wc, jnp.dot(lb, wa, precision=HIGH), precision=HIGH)
    zero = jnp.zeros_like(small)
    lower = jnp.block([[la, zero], [lb, lc]])
    inverse = jnp.block([[wa, zero], [wb, wc]])
    return lower, inverse


def from_two_sources(own, axis, sources):
    peers = lax.axis_size(axis)
    shape = own.shape
    flat = own.reshape(-1, shape[-1])
    spare = -flat.shape[0] % peers
    flat = jnp.pad(flat, [(0, spare), (0, 0)])
    pieces = flat.reshape(peers, -1, shape[-1])
    mine = lax.all_to_all(pieces, axis, 0, 0, tiled=False)
    kept = jnp.stack([mine[s] for s in sources])
    spread = lax.all_to_all(
        jnp.broadcast_to(kept[None], (peers, *kept.shape)), axis, 0, 0, tiled=False
    )
    whole = jnp.swapaxes(spread, 0, 1).reshape(len(sources), -1, shape[-1])
    whole = whole[:, : flat.shape[0] - spare]
    return whole.reshape(len(sources), *shape)


def on_device(kernel):
    prow = lax.axis_index("prow")
    pcol = lax.axis_index("pcol")
    rows = lax.axis_size("prow")
    cols = lax.axis_size("pcol")
    lbr, blk, lbc = kernel.shape[0], kernel.shape[2], kernel.shape[3]
    work = kernel.reshape(lbr, blk, lbc, blk)
    eye = jnp.eye(blk, dtype=jnp.float32)

    top = work[0]
    top_first = top[:, 0, :].reshape(rows, -1, blk)
    top_rest = jnp.swapaxes(top[:, 1:, :], 0, 1).reshape(rows, -1, blk)
    split = top_first.shape[1]
    top_mine = lax.all_to_all(
        jnp.concatenate([top_first, top_rest], axis=1), "prow", 0, 0, tiled=False
    )
    top_kept = jnp.stack([top_mine[0], top_mine[1]])
    top_spread = lax.all_to_all(
        jnp.broadcast_to(top_kept[None, :, :split], (rows, 2, split, blk)),
        "prow", 0, 0, tiled=False,
    )
    y_first = jnp.swapaxes(top_spread, 0, 1).reshape(2, blk, blk)
    y0c = y_first[0]
    y1c = y_first[1]
    top_gathered = lax.all_gather(top_kept[:, split:], "prow", axis=0, tiled=False)
    y_rest = jnp.swapaxes(top_gathered, 0, 1).reshape(2, lbc - 1, blk, blk)
    ytop = jnp.concatenate([y_first[:, None], y_rest], axis=1).transpose(0, 2, 1, 3)

    panel = work[:, :, 0, :].reshape(cols, -1, blk)
    panel_mine = lax.all_to_all(panel, "pcol", 0, 0, tiled=False)
    panel_kept = jnp.stack([panel_mine[0], panel_mine[1]])
    gathered = lax.all_gather(panel_kept, "pcol", axis=0, tiled=False)
    xs = jnp.swapaxes(gathered, 0, 1).reshape(2, lbr, blk, blk)
    x0 = xs[0]
    x1 = xs[1]

    extra = jnp.where(pcol == 0, jnp.stack([y0c, y1c]), jnp.stack([y1c, jnp.zeros_like(y1c)]))
    corner = from_two_sources(extra, "pcol", (0, 1))
    m00 = corner[0, 0]
    m10 = corner[0, 1]
    m11 = corner[1, 0]

    l0, w0 = chol_and_inverse(m00, eye)
    p10 = jnp.dot(m10, w0.T, precision=HIGH)
    s11 = m11 - jnp.dot(p10, p10.T, precision=HIGH)
    l1, w1 = chol_and_inverse(s11, eye)

    r0 = jnp.einsum("aik,jk->aij", x0, w0, precision=HIGH)
    r1 = x1 - jnp.einsum("aik,jk->aij", r0, p10, precision=HIGH)
    r1 = jnp.einsum("aik,jk->aij", r1, w1, precision=HIGH)

    c0t = jnp.einsum("ik,kbj->bij", w0, ytop[0], precision=HIGH)
    c1t = jnp.transpose(ytop[1], (1, 0, 2)) - jnp.einsum(
        "ik,bkj->bij", p10, c0t, precision=HIGH
    )
    c1t = jnp.einsum("ik,bkj->bij", w1, c1t, precision=HIGH)

    left = jnp.concatenate([r0, r1], axis=2)
    right = jnp.concatenate([c0t, c1t], axis=1)
    trailing = work - jnp.einsum("aik,bkj->aibj", left, right, precision=HIGH)

    row_ids = jnp.arange(lbr, dtype=jnp.int32) * rows + prow
    col_ids = jnp.arange(lbc, dtype=jnp.int32) * cols + pcol
    rk = row_ids[:, None, None]
    col0 = jnp.where(rk == 0, l0[None], r0)
    col1 = jnp.where(rk == 0, 0.0, jnp.where(rk == 1, l1[None], r1))
    first_col = jnp.where(pcol == 0, col0, jnp.where(pcol == 1, col1, trailing[:, :, 0, :]))
    out = trailing.at[:, :, 0, :].set(first_col)
    upper = (prow < 2) & (col_ids > prow)
    out = out.at[0].set(jnp.where(upper[None, :, None], 0.0, out[0]))
    return out.reshape(kernel.shape)


def solution(mesh):
    spec = P(None, "prow", None, None, "pcol", None)
    return jax.shard_map(
        on_device, mesh=mesh, in_specs=(spec,), out_specs=spec, check_vma=False
    )
```

```python
import jax
import jax.numpy as jnp
from jax import lax
from jax.sharding import PartitionSpec as P

HIGH = lax.Precision.HIGHEST


def chol_and_inverse(block, eye):
    h = block.shape[0] // 2
    small = eye[:h, :h]
    la = jnp.linalg.cholesky(block[:h, :h], symmetrize_input=False)
    wa = jax.scipy.linalg.solve_triangular(la, small, lower=True)
    lb = jnp.dot(block[h:, :h], wa.T, precision=HIGH)
    lc = jnp.linalg.cholesky(
        block[h:, h:] - jnp.dot(lb, lb.T, precision=HIGH), symmetrize_input=False
    )
    wc = jax.scipy.linalg.solve_triangular(lc, small, lower=True)
    wb = -jnp.dot(wc, jnp.dot(lb, wa, precision=HIGH), precision=HIGH)
    zero = jnp.zeros_like(small)
    lower = jnp.block([[la, zero], [lb, lc]])
    inverse = jnp.block([[wa, zero], [wb, wc]])
    return lower, inverse


def from_two_sources(own, axis, sources):
    peers = lax.axis_size(axis)
    shape = own.shape
    flat = own.reshape(-1, shape[-1])
    spare = -flat.shape[0] % peers
    flat = jnp.pad(flat, [(0, spare), (0, 0)])
    pieces = flat.reshape(peers, -1, shape[-1])
    mine = lax.all_to_all(pieces, axis, 0, 0, tiled=False)
    kept = jnp.stack([mine[s] for s in sources])
    spread = lax.all_to_all(
        jnp.broadcast_to(kept[None], (peers, *kept.shape)), axis, 0, 0, tiled=False
    )
    whole = jnp.swapaxes(spread, 0, 1).reshape(len(sources), -1, shape[-1])
    whole = whole[:, : flat.shape[0] - spare]
    return whole.reshape(len(sources), *shape)


def on_device(kernel):
    prow = lax.axis_index("prow")
    pcol = lax.axis_index("pcol")
    rows = lax.axis_size("prow")
    cols = lax.axis_size("pcol")
    lbr, blk, lbc = kernel.shape[0], kernel.shape[2], kernel.shape[3]
    work = kernel.reshape(lbr, blk, lbc, blk)
    eye = jnp.eye(blk, dtype=jnp.float32)

    top = work[0]
    top_first = top[:, 0, :].reshape(rows, -1, blk)
    top_rest = jnp.swapaxes(top[:, 1:, :], 0, 1).reshape(rows, -1, blk)
    split = top_first.shape[1]
    top_mine = lax.all_to_all(
        jnp.concatenate([top_first, top_rest], axis=1), "prow", 0, 0, tiled=False
    )
    top_kept = jnp.stack([top_mine[0], top_mine[1]])
    top_spread = lax.all_to_all(
        jnp.broadcast_to(top_kept[None, :, :split], (rows, 2, split, blk)),
        "prow", 0, 0, tiled=False,
    )
    y_first = jnp.swapaxes(top_spread, 0, 1).reshape(2, blk, blk)
    y0c = y_first[0]
    y1c = y_first[1]
    top_gathered = lax.all_gather(top_kept[:, split:], "prow", axis=0, tiled=False)
    y_rest = jnp.swapaxes(top_gathered, 0, 1).reshape(2, lbc - 1, blk, blk)
    ytop = jnp.concatenate([y_first[:, None], y_rest], axis=1).transpose(0, 2, 1, 3)

    extra = jnp.where(pcol == 0, jnp.stack([y0c, y1c]), jnp.stack([y1c, jnp.zeros_like(y1c)]))
    panel = work[:, :, 0, :].reshape(cols, -1, blk)
    extra_pieces = extra.reshape(cols, -1, blk)
    cut = panel.shape[1]
    pieces = jnp.concatenate([panel, extra_pieces], axis=1)
    mine = lax.all_to_all(pieces, "pcol", 0, 0, tiled=False)
    kept = jnp.stack([mine[0], mine[1]])
    spread = lax.all_to_all(
        jnp.broadcast_to(kept[None, :, cut:], (cols, 2, kept.shape[1] - cut, blk)),
        "pcol", 0, 0, tiled=False,
    )
    corner = jnp.swapaxes(spread, 0, 1).reshape(2, 2, blk, blk)
    m00 = corner[0, 0]
    m10 = corner[0, 1]
    m11 = corner[1, 0]
    gathered = lax.all_gather(kept[:, :cut], "pcol", axis=0, tiled=False)
    xs = jnp.swapaxes(gathered, 0, 1).reshape(2, lbr, blk, blk)
    x0 = xs[0]
    x1 = xs[1]

    def factor_step(k, carry):
        block, lowers, inverses, panels = carry
        lower, inverse = chol_and_inverse(block, eye)
        panel = jnp.dot(m10, inverse.T, precision=HIGH)
        nxt = m11 - jnp.dot(panel, panel.T, precision=HIGH)
        return (
            nxt,
            lowers.at[k].set(lower),
            inverses.at[k].set(inverse),
            panels.at[k].set(panel),
        )

    stacked = jnp.zeros((2, blk, blk), jnp.float32)
    _, lowers, inverses, panels = lax.fori_loop(
        0, 2, factor_step, (m00, stacked, stacked, stacked)
    )
    l0, w0, p10 = lowers[0], inverses[0], panels[0]
    l1, w1 = lowers[1], inverses[1]

    r0 = jnp.einsum("aik,jk->aij", x0, w0, precision=HIGH)
    r1 = x1 - jnp.einsum("aik,jk->aij", r0, p10, precision=HIGH)
    r1 = jnp.einsum("aik,jk->aij", r1, w1, precision=HIGH)

    c0t = jnp.einsum("ik,kbj->bij", w0, ytop[0], precision=HIGH)
    c1t = jnp.transpose(ytop[1], (1, 0, 2)) - jnp.einsum(
        "ik,bkj->bij", p10, c0t, precision=HIGH
    )
    c1t = jnp.einsum("ik,bkj->bij", w1, c1t, precision=HIGH)

    left = jnp.concatenate([r0, r1], axis=2)
    right = jnp.concatenate([c0t, c1t], axis=1)
    trailing = work - jnp.einsum("aik,bkj->aibj", left, right, precision=HIGH)

    row_ids = jnp.arange(lbr, dtype=jnp.int32) * rows + prow
    col_ids = jnp.arange(lbc, dtype=jnp.int32) * cols + pcol
    rk = row_ids[:, None, None]
    col0 = jnp.where(rk == 0, l0[None], r0)
    col1 = jnp.where(rk == 0, 0.0, jnp.where(rk == 1, l1[None], r1))
    first_col = jnp.where(pcol == 0, col0, jnp.where(pcol == 1, col1, trailing[:, :, 0, :]))
    out = trailing.at[:, :, 0, :].set(first_col)
    upper = (prow < 2) & (col_ids > prow)
    out = out.at[0].set(jnp.where(upper[None, :, None], 0.0, out[0]))
    return out.reshape(kernel.shape)


def solution(mesh):
    spec = P(None, "prow", None, None, "pcol", None)
    return jax.shard_map(
        on_device, mesh=mesh, in_specs=(spec,), out_specs=spec, check_vma=False
    )
```

```python
import jax
import jax.numpy as jnp
from jax import lax
from jax.sharding import PartitionSpec as P

HIGH = lax.Precision.HIGHEST


def chol_and_inverse(block, eye):
    h = block.shape[0] // 2
    small = eye[:h, :h]
    la = jnp.linalg.cholesky(block[:h, :h], symmetrize_input=False)
    wa = jax.scipy.linalg.solve_triangular(la, small, lower=True)
    lb = jnp.dot(block[h:, :h], wa.T, precision=HIGH)
    lc = jnp.linalg.cholesky(
        block[h:, h:] - jnp.dot(lb, lb.T, precision=HIGH), symmetrize_input=False
    )
    wc = jax.scipy.linalg.solve_triangular(lc, small, lower=True)
    wb = -jnp.dot(wc, jnp.dot(lb, wa, precision=HIGH), precision=HIGH)
    zero = jnp.zeros_like(small)
    lower = jnp.block([[la, zero], [lb, lc]])
    inverse = jnp.block([[wa, zero], [wb, wc]])
    return lower, inverse


def from_two_sources(own, axis, sources):
    peers = lax.axis_size(axis)
    shape = own.shape
    flat = own.reshape(-1, shape[-1])
    spare = -flat.shape[0] % peers
    flat = jnp.pad(flat, [(0, spare), (0, 0)])
    pieces = flat.reshape(peers, -1, shape[-1])
    mine = lax.all_to_all(pieces, axis, 0, 0, tiled=False)
    kept = jnp.stack([mine[s] for s in sources])
    spread = lax.all_to_all(
        jnp.broadcast_to(kept[None], (peers, *kept.shape)), axis, 0, 0, tiled=False
    )
    whole = jnp.swapaxes(spread, 0, 1).reshape(len(sources), -1, shape[-1])
    whole = whole[:, : flat.shape[0] - spare]
    return whole.reshape(len(sources), *shape)


def on_device(kernel):
    prow = lax.axis_index("prow")
    pcol = lax.axis_index("pcol")
    rows = lax.axis_size("prow")
    cols = lax.axis_size("pcol")
    lbr, blk, lbc = kernel.shape[0], kernel.shape[2], kernel.shape[3]
    work = kernel.reshape(lbr, blk, lbc, blk)
    eye = jnp.eye(blk, dtype=jnp.float32)

    top = work[0]
    top_first = top[:, 0, :].reshape(rows, -1, blk)
    top_rest = jnp.swapaxes(top[:, 1:, :], 0, 1).reshape(rows, -1, blk)
    split = top_first.shape[1]
    top_mine = lax.all_to_all(
        jnp.concatenate([top_first, top_rest], axis=1), "prow", 0, 0, tiled=False
    )
    top_kept = jnp.stack([top_mine[0], top_mine[1]])
    top_spread = lax.all_to_all(
        jnp.broadcast_to(top_kept[None, :, :split], (rows, 2, split, blk)),
        "prow", 0, 0, tiled=False,
    )
    y_first = jnp.swapaxes(top_spread, 0, 1).reshape(2, blk, blk)
    y0c = y_first[0]
    y1c = y_first[1]
    top_gathered = lax.all_gather(top_kept[:, split:], "prow", axis=0, tiled=False)
    y_rest = jnp.swapaxes(top_gathered, 0, 1).reshape(2, lbc - 1, blk, blk)
    ytop = jnp.concatenate([y_first[:, None], y_rest], axis=1).transpose(0, 2, 1, 3)

    extra = jnp.where(pcol == 0, jnp.stack([y0c, y1c]), jnp.stack([y1c, jnp.zeros_like(y1c)]))
    panel = work[:, :, 0, :].reshape(cols, -1, blk)
    extra_pieces = extra.reshape(cols, -1, blk)
    cut = panel.shape[1]
    pieces = jnp.concatenate([panel, extra_pieces], axis=1)
    mine = lax.all_to_all(pieces, "pcol", 0, 0, tiled=False)
    kept = jnp.stack([mine[0], mine[1]])
    spread = lax.all_to_all(
        jnp.broadcast_to(kept[None, :, cut:], (cols, 2, kept.shape[1] - cut, blk)),
        "pcol", 0, 0, tiled=False,
    )
    corner = jnp.swapaxes(spread, 0, 1).reshape(2, 2, blk, blk)
    m00 = corner[0, 0]
    m10 = corner[0, 1]
    m11 = corner[1, 0]
    gathered = lax.all_gather(kept[:, :cut], "pcol", axis=0, tiled=False)
    xs = jnp.swapaxes(gathered, 0, 1).reshape(2, lbr, blk, blk)
    x0 = xs[0]
    x1 = xs[1]

    def factor_step(k, carry):
        block, lowers, inverses, panels = carry
        lower, inverse = chol_and_inverse(block, eye)
        def next_block(w):
            panel = jnp.dot(m10, w.T, precision=HIGH)
            return m11 - jnp.dot(panel, panel.T, precision=HIGH), panel

        nxt, panel = lax.cond(
            k == 0, next_block, lambda w: (block, jnp.zeros_like(block)), inverse
        )
        return (
            nxt,
            lowers.at[k].set(lower),
            inverses.at[k].set(inverse),
            panels.at[k].set(panel),
        )

    stacked = jnp.zeros((2, blk, blk), jnp.float32)
    _, lowers, inverses, panels = lax.fori_loop(
        0, 2, factor_step, (m00, stacked, stacked, stacked)
    )
    l0, w0, p10 = lowers[0], inverses[0], panels[0]
    l1, w1 = lowers[1], inverses[1]

    r0 = jnp.einsum("aik,jk->aij", x0, w0, precision=HIGH)
    r1 = x1 - jnp.einsum("aik,jk->aij", r0, p10, precision=HIGH)
    r1 = jnp.einsum("aik,jk->aij", r1, w1, precision=HIGH)

    c0t = jnp.einsum("ik,kbj->bij", w0, ytop[0], precision=HIGH)
    c1t = jnp.transpose(ytop[1], (1, 0, 2)) - jnp.einsum(
        "ik,bkj->bij", p10, c0t, precision=HIGH
    )
    c1t = jnp.einsum("ik,bkj->bij", w1, c1t, precision=HIGH)

    left = jnp.concatenate([r0, r1], axis=2)
    right = jnp.concatenate([c0t, c1t], axis=1)
    trailing = work - jnp.einsum("aik,bkj->aibj", left, right, precision=HIGH)

    row_ids = jnp.arange(lbr, dtype=jnp.int32) * rows + prow
    col_ids = jnp.arange(lbc, dtype=jnp.int32) * cols + pcol
    rk = row_ids[:, None, None]
    col0 = jnp.where(rk == 0, l0[None], r0)
    col1 = jnp.where(rk == 0, 0.0, jnp.where(rk == 1, l1[None], r1))
    first_col = jnp.where(pcol == 0, col0, jnp.where(pcol == 1, col1, trailing[:, :, 0, :]))
    out = trailing.at[:, :, 0, :].set(first_col)
    upper = (prow < 2) & (col_ids > prow)
    out = out.at[0].set(jnp.where(upper[None, :, None], 0.0, out[0]))
    return out.reshape(kernel.shape)


def solution(mesh):
    spec = P(None, "prow", None, None, "pcol", None)
    return jax.shard_map(
        on_device, mesh=mesh, in_specs=(spec,), out_specs=spec, check_vma=False
    )
```

```python
import jax
import jax.numpy as jnp
from jax import lax
from jax.sharding import PartitionSpec as P

HIGH = lax.Precision.HIGHEST


def chol_and_inverse(block, eye):
    h = block.shape[0] // 2
    small = eye[:h, :h]
    la = jnp.linalg.cholesky(block[:h, :h], symmetrize_input=False)
    wa = jax.scipy.linalg.solve_triangular(la, small, lower=True)
    lb = jnp.dot(block[h:, :h], wa.T, precision=HIGH)
    lc = jnp.linalg.cholesky(
        block[h:, h:] - jnp.dot(lb, lb.T, precision=HIGH), symmetrize_input=False
    )
    wc = jax.scipy.linalg.solve_triangular(lc, small, lower=True)
    wb = -jnp.dot(wc, jnp.dot(lb, wa, precision=HIGH), precision=HIGH)
    zero = jnp.zeros_like(small)
    lower = jnp.block([[la, zero], [lb, lc]])
    inverse = jnp.block([[wa, zero], [wb, wc]])
    return lower, inverse


def from_two_sources(own, axis, sources):
    peers = lax.axis_size(axis)
    shape = own.shape
    flat = own.reshape(-1, shape[-1])
    spare = -flat.shape[0] % peers
    flat = jnp.pad(flat, [(0, spare), (0, 0)])
    pieces = flat.reshape(peers, -1, shape[-1])
    mine = lax.all_to_all(pieces, axis, 0, 0, tiled=False)
    kept = jnp.stack([mine[s] for s in sources])
    spread = lax.all_to_all(
        jnp.broadcast_to(kept[None], (peers, *kept.shape)), axis, 0, 0, tiled=False
    )
    whole = jnp.swapaxes(spread, 0, 1).reshape(len(sources), -1, shape[-1])
    whole = whole[:, : flat.shape[0] - spare]
    return whole.reshape(len(sources), *shape)


def on_device(kernel):
    prow = lax.axis_index("prow")
    pcol = lax.axis_index("pcol")
    rows = lax.axis_size("prow")
    cols = lax.axis_size("pcol")
    lbr, blk, lbc = kernel.shape[0], kernel.shape[2], kernel.shape[3]
    work = kernel.reshape(lbr, blk, lbc, blk)
    eye = jnp.eye(blk, dtype=jnp.float32)

    top = work[0]
    top_rows = jnp.swapaxes(top, 0, 1).reshape(-1, blk)
    half = top_rows.shape[0] // 2
    top_first = top_rows[:half].reshape(rows, -1, blk)
    top_rest = top_rows[half:].reshape(rows, -1, blk)
    split = top_first.shape[1]
    top_mine = lax.all_to_all(
        jnp.concatenate([top_first, top_rest], axis=1), "prow", 0, 0, tiled=False
    )
    top_kept = jnp.stack([top_mine[0], top_mine[1]])
    top_spread = lax.all_to_all(
        jnp.broadcast_to(top_kept[None, :, :split], (rows, 2, split, blk)),
        "prow", 0, 0, tiled=False,
    )
    y_first = jnp.swapaxes(top_spread, 0, 1).reshape(2, -1, blk)
    y0c = y_first[0, :blk]
    y1c = y_first[1, :blk]
    top_gathered = lax.all_gather(top_kept[:, split:], "prow", axis=0, tiled=False)
    y_rest = jnp.swapaxes(top_gathered, 0, 1).reshape(2, -1, blk)
    ytop = jnp.concatenate([y_first, y_rest], axis=1).reshape(2, lbc, blk, blk)
    ytop = ytop.transpose(0, 2, 1, 3)

    extra = jnp.where(pcol == 0, jnp.stack([y0c, y1c]), jnp.stack([y1c, jnp.zeros_like(y1c)]))
    panel = work[:, :, 0, :].reshape(cols, -1, blk)
    extra_pieces = extra.reshape(cols, -1, blk)
    cut = panel.shape[1]
    pieces = jnp.concatenate([panel, extra_pieces], axis=1)
    mine = lax.all_to_all(pieces, "pcol", 0, 0, tiled=False)
    kept = jnp.stack([mine[0], mine[1]])
    spread = lax.all_to_all(
        jnp.broadcast_to(kept[None, :, cut:], (cols, 2, kept.shape[1] - cut, blk)),
        "pcol", 0, 0, tiled=False,
    )
    corner = jnp.swapaxes(spread, 0, 1).reshape(2, 2, blk, blk)
    m00 = corner[0, 0]
    m10 = corner[0, 1]
    m11 = corner[1, 0]
    gathered = lax.all_gather(kept[:, :cut], "pcol", axis=0, tiled=False)
    xs = jnp.swapaxes(gathered, 0, 1).reshape(2, lbr, blk, blk)
    x0 = xs[0]
    x1 = xs[1]

    def factor_step(k, carry):
        block, lowers, inverses, panels = carry
        lower, inverse = chol_and_inverse(block, eye)
        panel = jnp.dot(m10, inverse.T, precision=HIGH)
        nxt = m11 - jnp.dot(panel, panel.T, precision=HIGH)
        return (
            nxt,
            lowers.at[k].set(lower),
            inverses.at[k].set(inverse),
            panels.at[k].set(panel),
        )

    stacked = jnp.zeros((2, blk, blk), jnp.float32)
    _, lowers, inverses, panels = lax.fori_loop(
        0, 2, factor_step, (m00, stacked, stacked, stacked)
    )
    l0, w0, p10 = lowers[0], inverses[0], panels[0]
    l1, w1 = lowers[1], inverses[1]

    r0 = jnp.einsum("aik,jk->aij", x0, w0, precision=HIGH)
    r1 = x1 - jnp.einsum("aik,jk->aij", r0, p10, precision=HIGH)
    r1 = jnp.einsum("aik,jk->aij", r1, w1, precision=HIGH)

    c0t = jnp.einsum("ik,kbj->bij", w0, ytop[0], precision=HIGH)
    c1t = jnp.transpose(ytop[1], (1, 0, 2)) - jnp.einsum(
        "ik,bkj->bij", p10, c0t, precision=HIGH
    )
    c1t = jnp.einsum("ik,bkj->bij", w1, c1t, precision=HIGH)

    left = jnp.concatenate([r0, r1], axis=2)
    right = jnp.concatenate([c0t, c1t], axis=1)
    trailing = work - jnp.einsum("aik,bkj->aibj", left, right, precision=HIGH)

    row_ids = jnp.arange(lbr, dtype=jnp.int32) * rows + prow
    col_ids = jnp.arange(lbc, dtype=jnp.int32) * cols + pcol
    rk = row_ids[:, None, None]
    col0 = jnp.where(rk == 0, l0[None], r0)
    col1 = jnp.where(rk == 0, 0.0, jnp.where(rk == 1, l1[None], r1))
    first_col = jnp.where(pcol == 0, col0, jnp.where(pcol == 1, col1, trailing[:, :, 0, :]))
    out = trailing.at[:, :, 0, :].set(first_col)
    upper = (prow < 2) & (col_ids > prow)
    out = out.at[0].set(jnp.where(upper[None, :, None], 0.0, out[0]))
    return out.reshape(kernel.shape)


def solution(mesh):
    spec = P(None, "prow", None, None, "pcol", None)
    return jax.shard_map(
        on_device, mesh=mesh, in_specs=(spec,), out_specs=spec, check_vma=False
    )
```
